512 devices in a mesh: rep: 64 (over z, x_lo, core), tile: 8 (over y, x_hi).
Axes of the slice: x: 4 (x_hi: 2, x_lo: 2; x = x_hi * 2 + x_lo), y: 4, z: 16, core: 2. Of those that a mesh axis runs over, the one named last changes fastest.
Arguments:
- images: bfloat16 [2, 64, 1, 16, 256, 128], P(None, 'rep', None, 'tile'), may hold values from -12 to 12
- out_grads: bfloat16 [2, 64, 1, 16, 256, 128], P(None, 'rep', None, 'tile'), may hold values from -12 to 12
- numerators: float32 [64, 2, 1152, 128], P('rep'), may hold values from -5 to 5
- push_weight: float32 [64], P('rep'), may hold values from 0.5 to 2
- step_index: int32 [1], replicated, may hold values from 0 to 999
Outputs:
- new_numerators: float32 [64, 2, 1152, 128], P('rep')
- new_weight: float32 [64], P('rep')
The draws below stay inside these ranges and needn't reach their ends.
Inputs may be any that keep to these rules, and one draw needn't show every extreme that they name: Step s of the window pairs replica r with replica r - 2 ** ((step_index + s) mod log2 64).
All inputs are finite; a program needn't handle non-finite values.
Results may differ from the reference program's by a relative error of at most 0.01.
Values may be sent and summed in bfloat16 or wider, within the bound.
No kernel may reach another device: no remote copies, remote signals or barrier semaphores. Data moves between devices by JAX's collectives and lax.ppermute only.
A program may use at most 64 MiB of HBM per device.

```python
import math
import jax
import jax.numpy as jnp
from jax import lax

CH = 128
WIDTH = 256
BATCH = 1
STEPS = 2
REPS = 64
CROP_ROWS = 16


def block_levels(key, shape, shards, low, largest):
    def one(dim, parts):
        draws = jax.random.uniform(jax.random.fold_in(jax.random.fold_in(key, 6), dim), (parts,), jnp.float32, low / len(shards), largest / len(shards))
        return jnp.repeat(jnp.exp(draws), shape[dim] // parts).reshape((-1,) + (1,) * (len(shape) - dim - 1))

    level = one(*shards[0])
    for cut in shards[1:]:
        level = level * one(*cut)
    return level


def bell_draw(key, shape, spread, reach, cuts=(), kind=jnp.bfloat16):
    level = block_levels(key, shape, cuts, -0.22, 0.18) if cuts else 1.0
    entries = jax.random.normal(key, shape, jnp.float32) * spread * level
    return jnp.minimum(jnp.maximum(entries, -reach), reach).astype(kind)


def setup_inputs(seed: int = 0) -> dict:
    arg_keys = jax.random.split(jax.random.key(seed), 6)
    return {
        "images": bell_draw(arg_keys[0], (STEPS, REPS, BATCH, CROP_ROWS, WIDTH, CH), 3.0, 12.0, ((1, 64), (3, 8))),
        "out_grads": bell_draw(arg_keys[1], (STEPS, REPS, BATCH, CROP_ROWS, WIDTH, CH), 3.0, 12.0, ((1, 64), (3, 8))),
        "numerators": bell_draw(arg_keys[2], (REPS, 2, 9 * CH, CH), 1.0, 5.0, ((0, 64),), jnp.float32),
        "push_weight": jnp.clip(jnp.exp(math.log(2.0) - 1.3862944 * jax.random.uniform(arg_keys[3], (REPS,), jnp.float32) ** block_levels(arg_keys[3], (REPS,), ((0, 64),), -0.2, 0.2)), 0.5, 2.0),
        "step_index": jax.random.randint(arg_keys[4], (1,), 0, 1000).astype(jnp.int32),
    }


learn_rate = 0.03

def pad_all(field_in):
    return jnp.pad(field_in, ((0, 0), (1, 1), (1, 1), (0, 0)))

def patches(padded):
    out_rows = padded.shape[1] - 2
    out_cols = padded.shape[2] - 2
    pieces = [padded[:, row_off:row_off + out_rows, col_off:col_off + out_cols, :] for row_off in range(3) for col_off in range(3)]
    return jnp.concatenate(pieces, axis=-1).reshape(-1, 9 * padded.shape[3])

def flipped(kernel):
    channels = kernel.shape[1]
    return kernel.reshape(3, 3, channels, channels)[::-1, ::-1].transpose(0, 1, 3, 2).reshape(9 * channels, channels)

def contract_rows(left_mat, right_mat):
    return lax.dot_general(left_mat, right_mat, (((0,), (0,)), ((), ())), preferred_element_type=jnp.float32)

def replica_grads(operands):
    inputs, out_grad, weights = operands
    channels = inputs.shape[-1]
    norm_scale = 1.0 / math.sqrt(9 * channels)
    input_patches = patches(pad_all(inputs))
    pre_act = norm_scale * jnp.dot(input_patches, weights[0], preferred_element_type=jnp.float32)
    hidden = jax.nn.silu(pre_act).astype(jnp.bfloat16).reshape(inputs.shape)
    hidden_patches = patches(pad_all(hidden))
    grad_patches = patches(pad_all(out_grad))
    grad_hidden = norm_scale * jnp.dot(grad_patches, flipped(weights[1]), preferred_element_type=jnp.float32)
    sigmoid_val = jax.nn.sigmoid(pre_act)
    grad_pre = (grad_hidden * sigmoid_val * (1.0 + pre_act * (1.0 - sigmoid_val))).astype(jnp.bfloat16)
    first_grad = norm_scale * contract_rows(input_patches, grad_pre)
    second = norm_scale * contract_rows(hidden_patches, out_grad.reshape(-1, channels))
    return jnp.stack([first_grad, second])

def reference(images, out_grads, numerators, push_weight, step_index):
    levels = REPS.bit_length() - 1
    sum_state = numerators
    weight = push_weight
    for step_num in range(STEPS):
        weights = (sum_state / weight[:, None, None, None]).astype(jnp.bfloat16)
        local_grads = lax.map(replica_grads, (images[step_num], out_grads[step_num], weights))
        sum_state = sum_state - learn_rate * local_grads
        peer_level = ((step_index[0] + step_num) % levels).astype(jnp.int32)
        offset = jnp.left_shift(jnp.int32(1), peer_level)
        sum_state = 0.5 * (sum_state + jnp.roll(sum_state, offset, axis=0))
        weight = 0.5 * (weight + jnp.roll(weight, offset, axis=0))
    return (sum_state, weight)
```

```python
from functools import partial
import math

import jax
import jax.numpy as jnp
from jax import lax
from jax.sharding import PartitionSpec as P

learn_rate = 0.03


def passed_along(shard, axis, by):
    devices = lax.axis_size(axis)
    return lax.ppermute(shard, axis, [(i, (i + by) % devices) for i in range(devices)])


def pushed(payload, level):
    levels = lax.axis_size("rep").bit_length() - 1
    branches = [partial(passed_along, axis="rep", by=1 << bit_num) for bit_num in range(levels)]
    return lax.switch(level, branches, payload)


def pad_columns(field_in):
    return jnp.pad(field_in, ((0, 0), (0, 0), (1, 1), (0, 0)))


def patches(padded):
    out_rows = padded.shape[1] - 2
    out_cols = padded.shape[2] - 2
    pieces = [
        padded[:, row_off : row_off + out_rows, col_off : col_off + out_cols, :]
        for row_off in range(3)
        for col_off in range(3)
    ]
    return jnp.concatenate(pieces, axis=-1).reshape(-1, 9 * padded.shape[3])


def flipped(kernel):
    channels = kernel.shape[1]
    return (
        kernel.reshape(3, 3, channels, channels)[::-1, ::-1]
        .transpose(0, 1, 3, 2)
        .reshape(9 * channels, channels)
    )


def contract_rows(left_mat, right_mat):
    return lax.dot_general(
        left_mat, right_mat, (((0,), (0,)), ((), ())), preferred_element_type=jnp.float32
    )


def halo_rows(images, out_grads):
    tiles = lax.axis_size("tile")
    own_rows = images.shape[3]
    for_below = jnp.concatenate([images[:, 0], out_grads[:, 0, :, own_rows - 1 :]], axis=2)
    for_above = jnp.concatenate([images[:, 0], out_grads[:, 0, :, :1]], axis=2)
    down = [(i, i + 1) for i in range(tiles - 1)]
    up = [(i + 1, i) for i in range(tiles - 1)]
    return lax.ppermute(for_below, "tile", down), lax.ppermute(for_above, "tile", up)


def local_grads(x_ext, g_ext, weights, first, last):
    batch_size, ext_rows, columns, channels = x_ext.shape
    own_rows = ext_rows - 4
    norm_scale = 1.0 / math.sqrt(9 * channels)
    input_patches = patches(pad_columns(x_ext))
    pre_ext = norm_scale * jnp.dot(input_patches, weights[0], preferred_element_type=jnp.float32)
    pre_ext = pre_ext.reshape(batch_size, own_rows + 2, columns, channels)
    row_ids = lax.broadcasted_iota(jnp.int32, (1, own_rows + 2, 1, 1), 1)
    outside = ((row_ids == 0) & first) | ((row_ids == own_rows + 1) & last)
    hidden_ext = jnp.where(outside, 0.0, jax.nn.silu(pre_ext)).astype(jnp.bfloat16)
    pre_act = pre_ext[:, 1 : own_rows + 1].reshape(-1, channels)
    own_input_patches = input_patches.reshape(batch_size, own_rows + 2, columns, -1)[
        :, 1 : own_rows + 1
    ].reshape(-1, 9 * channels)
    hidden_patches = patches(pad_columns(hidden_ext))
    grad_patches = patches(pad_columns(g_ext))
    grad_hidden = norm_scale * jnp.dot(
        grad_patches, flipped(weights[1]), preferred_element_type=jnp.float32
    )
    sigmoid_val = jax.nn.sigmoid(pre_act)
    grad_pre = (grad_hidden * sigmoid_val * (1.0 + pre_act * (1.0 - sigmoid_val))).astype(
        jnp.bfloat16
    )
    grad_own = g_ext[:, 1 : own_rows + 1].reshape(-1, channels)
    first_grad = norm_scale * contract_rows(own_input_patches, grad_pre)
    second = norm_scale * contract_rows(hidden_patches, grad_own)
    return jnp.stack([first_grad, second])


def scattered_sum(grads, tiles):
    chunks = grads.astype(jnp.bfloat16).reshape(tiles, -1, grads.shape[-1])
    got = lax.all_to_all(chunks, "tile", 0, 0, tiled=True)
    return got.astype(jnp.float32).sum(0)


def gathered(chunk, tiles):
    spread = jnp.broadcast_to(chunk[None], (tiles,) + chunk.shape)
    return lax.all_to_all(spread, "tile", 0, 0, tiled=True)


def with_weight(chunk, weight):
    return jnp.concatenate([chunk, jnp.broadcast_to(weight, (1, chunk.shape[-1]))], axis=0)


def shards(images, out_grads, numerators, push_weight, step_index):
    levels = lax.axis_size("rep").bit_length() - 1
    tiles = lax.axis_size("tile")
    tile = lax.axis_index("tile")
    first, last = tile == 0, tile == tiles - 1
    kernel_shape = numerators.shape[1:]
    channels = kernel_shape[-1]
    full_state = numerators[0]
    state_rows = full_state.size // (tiles * channels)
    sum_state = full_state.reshape(tiles, state_rows, channels)[tile]
    weight = push_weight[0]
    above, below = halo_rows(images, out_grads)
    own_rows = images.shape[3]
    got = pushed(with_weight(sum_state, weight), step_index[0] % levels)
    for step_num in range(images.shape[0]):
        peer_level = (step_index[0] + step_num) % levels
        if step_num == 0:
            weights = (full_state / weight).astype(jnp.bfloat16)
        else:
            weights = gathered((sum_state / weight).astype(jnp.bfloat16), tiles).reshape(
                kernel_shape
            )
            got = pushed(with_weight(sum_state, weight), peer_level)
        x_ext = jnp.concatenate(
            [above[step_num][:, :own_rows], images[step_num, 0], below[step_num][:, :own_rows]],
            axis=1,
        )
        g_ext = jnp.concatenate(
            [above[step_num][:, own_rows:], out_grads[step_num, 0], below[step_num][:, own_rows:]],
            axis=1,
        )
        grads_chunk = scattered_sum(local_grads(x_ext, g_ext, weights, first, last), tiles)
        peer_grads = pushed(grads_chunk, peer_level)
        own_part = sum_state - learn_rate * grads_chunk
        peer_part = got[:state_rows] - learn_rate * peer_grads
        sum_state = 0.5 * (own_part + peer_part)
        weight = 0.5 * (weight + got[state_rows, 0])
    new_state = gathered(sum_state, tiles).reshape(kernel_shape)
    return (new_state[None], jnp.reshape(weight, (1,)))


def solution(mesh):
    in_specs = (
        P(None, "rep", None, "tile", None, None),
        P(None, "rep", None, "tile", None, None),
        P("rep", None, None, None),
        P("rep"),
        P(),
    )
    out_specs = (P("rep", None, None, None), P("rep"))
    return jax.shard_map(shards, mesh=mesh, in_specs=in_specs, out_specs=out_specs, check_vma=False)
```

```python
from functools import partial
import math

import jax
import jax.numpy as jnp
from jax import lax
from jax.sharding import PartitionSpec as P

learn_rate = 0.03


def passed_along(shard, axis, by):
    devices = lax.axis_size(axis)
    return lax.ppermute(shard, axis, [(i, (i + by) % devices) for i in range(devices)])


def pushed(payload, level):
    levels = lax.axis_size("rep").bit_length() - 1
    branches = [partial(passed_along, axis="rep", by=1 << bit_num) for bit_num in range(levels)]
    return lax.switch(level, branches, payload)


def pad_columns(field_in):
    return jnp.pad(field_in, ((0, 0), (0, 0), (1, 1), (0, 0)))


def patches(padded):
    out_rows = padded.shape[1] - 2
    out_cols = padded.shape[2] - 2
    pieces = [
        padded[:, row_off : row_off + out_rows, col_off : col_off + out_cols, :]
        for row_off in range(3)
        for col_off in range(3)
    ]
    return jnp.concatenate(pieces, axis=-1).reshape(-1, 9 * padded.shape[3])


def flipped(kernel):
    channels = kernel.shape[1]
    return (
        kernel.reshape(3, 3, channels, channels)[::-1, ::-1]
        .transpose(0, 1, 3, 2)
        .reshape(9 * channels, channels)
    )


def contract_rows(left_mat, right_mat):
    return lax.dot_general(
        left_mat, right_mat, (((0,), (0,)), ((), ())), preferred_element_type=jnp.float32
    )


def halo_rows(images, out_grads):
    tiles = lax.axis_size("tile")
    own_rows = images.shape[3]
    for_below = jnp.concatenate([images[:, 0], out_grads[:, 0, :, own_rows - 1 :]], axis=2)
    for_above = jnp.concatenate([images[:, 0], out_grads[:, 0, :, :1]], axis=2)
    down = [(i, i + 1) for i in range(tiles - 1)]
    up = [(i + 1, i) for i in range(tiles - 1)]
    return lax.ppermute(for_below, "tile", down), lax.ppermute(for_above, "tile", up)


def local_grads(x_ext, g_ext, weights, first, last):
    batch_size, ext_rows, columns, channels = x_ext.shape
    own_rows = ext_rows - 4
    norm_scale = 1.0 / math.sqrt(9 * channels)
    input_patches = patches(pad_columns(x_ext))
    pre_ext = norm_scale * jnp.dot(input_patches, weights[0], preferred_element_type=jnp.float32)
    pre_ext = pre_ext.reshape(batch_size, own_rows + 2, columns, channels)
    row_ids = lax.broadcasted_iota(jnp.int32, (1, own_rows + 2, 1, 1), 1)
    outside = ((row_ids == 0) & first) | ((row_ids == own_rows + 1) & last)
    hidden_ext = jnp.where(outside, 0.0, jax.nn.silu(pre_ext)).astype(jnp.bfloat16)
    pre_act = pre_ext[:, 1 : own_rows + 1].reshape(-1, channels)
    own_input_patches = input_patches.reshape(batch_size, own_rows + 2, columns, -1)[
        :, 1 : own_rows + 1
    ].reshape(-1, 9 * channels)
    hidden_patches = patches(pad_columns(hidden_ext))
    grad_patches = patches(pad_columns(g_ext))
    grad_hidden = norm_scale * jnp.dot(
        grad_patches, flipped(weights[1]), preferred_element_type=jnp.float32
    )
    sigmoid_val = jax.nn.sigmoid(pre_act)
    grad_pre = (grad_hidden * sigmoid_val * (1.0 + pre_act * (1.0 - sigmoid_val))).astype(
        jnp.bfloat16
    )
    grad_own = g_ext[:, 1 : own_rows + 1].reshape(-1, channels)
    first_grad = norm_scale * contract_rows(own_input_patches, grad_pre)
    second = norm_scale * contract_rows(hidden_patches, grad_own)
    return jnp.stack([first_grad, second])


def scattered_sum(grads, tiles):
    chunks = grads.astype(jnp.bfloat16).reshape(tiles, -1, grads.shape[-1])
    got = lax.all_to_all(chunks, "tile", 0, 0, tiled=True)
    return got.astype(jnp.float32).sum(0)


def gathered(chunk, tiles):
    spread = jnp.broadcast_to(chunk[None], (tiles,) + chunk.shape)
    return lax.all_to_all(spread, "tile", 0, 0, tiled=True)


def with_weight(chunk, weight):
    return jnp.concatenate([chunk, jnp.broadcast_to(weight, (1, chunk.shape[-1]))], axis=0)


def shards(images, out_grads, numerators, push_weight, step_index):
    levels = lax.axis_size("rep").bit_length() - 1
    tiles = lax.axis_size("tile")
    tile = lax.axis_index("tile")
    first, last = tile == 0, tile == tiles - 1
    kernel_shape = numerators.shape[1:]
    channels = kernel_shape[-1]
    full_state = numerators[0]
    state_rows = full_state.size // (tiles * channels)
    sum_state = full_state.reshape(tiles, state_rows, channels)[tile]
    weight = push_weight[0]
    above, below = halo_rows(images, out_grads)
    own_rows = images.shape[3]
    for step_num in range(images.shape[0]):
        peer_level = (step_index[0] + step_num) % levels
        if step_num == 0:
            weights = (full_state / weight).astype(jnp.bfloat16)
        else:
            weights = gathered((sum_state / weight).astype(jnp.bfloat16), tiles).reshape(
                kernel_shape
            )
        x_ext = jnp.concatenate(
            [above[step_num][:, :own_rows], images[step_num, 0], below[step_num][:, :own_rows]],
            axis=1,
        )
        g_ext = jnp.concatenate(
            [above[step_num][:, own_rows:], out_grads[step_num, 0], below[step_num][:, own_rows:]],
            axis=1,
        )
        grads_chunk = scattered_sum(local_grads(x_ext, g_ext, weights, first, last), tiles)
        sum_state = sum_state - learn_rate * grads_chunk
        got = pushed(with_weight(sum_state, weight), peer_level)
        sum_state = 0.5 * (sum_state + got[:state_rows])
        weight = 0.5 * (weight + got[state_rows, 0])
    new_state = gathered(sum_state, tiles).reshape(kernel_shape)
    return (new_state[None], jnp.reshape(weight, (1,)))


def solution(mesh):
    in_specs = (
        P(None, "rep", None, "tile", None, None),
        P(None, "rep", None, "tile", None, None),
        P("rep", None, None, None),
        P("rep"),
        P(),
    )
    out_specs = (P("rep", None, None, None), P("rep"))
    return jax.shard_map(shards, mesh=mesh, in_specs=in_specs, out_specs=out_specs, check_vma=False)
```

```python
from functools import partial
import math

import jax
import jax.numpy as jnp
from jax import lax
from jax.sharding import PartitionSpec as P

learn_rate = 0.03


def passed_along(shard, axis, by):
    devices = lax.axis_size(axis)
    return lax.ppermute(shard, axis, [(i, (i + by) % devices) for i in range(devices)])


def pushed(payload, level):
    levels = lax.axis_size("rep").bit_length() - 1
    branches = [partial(passed_along, axis="rep", by=1 << bit_num) for bit_num in range(levels)]
    return lax.switch(level, branches, payload)


def conv_rows(field, kernel):
    channels = kernel.shape[1]
    return lax.conv_general_dilated(
        field,
        kernel.reshape(3, 3, channels, channels),
        (1, 1),
        ((0, 0), (1, 1)),
        dimension_numbers=("NHWC", "HWIO", "NHWC"),
        preferred_element_type=jnp.float32,
    )


def flipped(kernel):
    channels = kernel.shape[1]
    return (
        kernel.reshape(3, 3, channels, channels)[::-1, ::-1]
        .transpose(0, 1, 3, 2)
        .reshape(9 * channels, channels)
    )


def kernel_grad(field, cotangent):
    padded = jnp.pad(field, ((0, 0), (0, 0), (1, 1), (0, 0)))
    out = lax.conv_general_dilated(
        padded,
        cotangent,
        (1, 1),
        "VALID",
        dimension_numbers=("CHWN", "IHWO", "NHWC"),
        preferred_element_type=jnp.float32,
    )
    return out.transpose(1, 2, 0, 3).reshape(-1, cotangent.shape[-1])


def halo_rows(images, out_grads):
    tiles = lax.axis_size("tile")
    own_rows = images.shape[3]
    for_below = jnp.concatenate([images[:, 0], out_grads[:, 0, :, own_rows - 1 :]], axis=2)
    for_above = jnp.concatenate([images[:, 0], out_grads[:, 0, :, :1]], axis=2)
    down = [(i, i + 1) for i in range(tiles - 1)]
    up = [(i + 1, i) for i in range(tiles - 1)]
    return lax.ppermute(for_below, "tile", down), lax.ppermute(for_above, "tile", up)


def local_grads(x_ext, g_ext, weights, first, last):
    channels = x_ext.shape[-1]
    own_rows = x_ext.shape[1] - 4
    norm_scale = 1.0 / math.sqrt(9 * channels)
    pre_ext = norm_scale * conv_rows(x_ext, weights[0])
    row_ids = lax.broadcasted_iota(jnp.int32, (1, own_rows + 2, 1, 1), 1)
    outside = ((row_ids == 0) & first) | ((row_ids == own_rows + 1) & last)
    hidden_ext = jnp.where(outside, 0.0, jax.nn.silu(pre_ext)).astype(jnp.bfloat16)
    pre_act = pre_ext[:, 1 : own_rows + 1]
    grad_hidden = norm_scale * conv_rows(g_ext, flipped(weights[1]))
    sigmoid_val = jax.nn.sigmoid(pre_act)
    grad_pre = (grad_hidden * sigmoid_val * (1.0 + pre_act * (1.0 - sigmoid_val))).astype(
        jnp.bfloat16
    )
    grad_own = g_ext[:, 1 : own_rows + 1]
    first_grad = norm_scale * kernel_grad(x_ext[:, 1 : own_rows + 3], grad_pre)
    second = norm_scale * kernel_grad(hidden_ext, grad_own)
    return jnp.stack([first_grad, second])


def scattered_sum(grads, tiles):
    chunks = grads.astype(jnp.bfloat16).reshape(tiles, -1, grads.shape[-1])
    got = lax.all_to_all(chunks, "tile", 0, 0, tiled=True)
    return got.astype(jnp.float32).sum(0)


def gathered(chunk, tiles):
    spread = jnp.broadcast_to(chunk[None], (tiles,) + chunk.shape)
    return lax.all_to_all(spread, "tile", 0, 0, tiled=True)


def with_weight(chunk, weight):
    return jnp.concatenate([chunk, jnp.broadcast_to(weight, (1, chunk.shape[-1]))], axis=0)


def shards(images, out_grads, numerators, push_weight, step_index):
    levels = lax.axis_size("rep").bit_length() - 1
    tiles = lax.axis_size("tile")
    tile = lax.axis_index("tile")
    first, last = tile == 0, tile == tiles - 1
    kernel_shape = numerators.shape[1:]
    channels = kernel_shape[-1]
    full_state = numerators[0]
    state_rows = full_state.size // (tiles * channels)
    sum_state = full_state.reshape(tiles, state_rows, channels)[tile]
    weight = push_weight[0]
    above, below = halo_rows(images, out_grads)
    own_rows = images.shape[3]
    for step_num in range(images.shape[0]):
        peer_level = (step_index[0] + step_num) % levels
        if step_num == 0:
            weights = (full_state / weight).astype(jnp.bfloat16)
        else:
            weights = gathered((sum_state / weight).astype(jnp.bfloat16), tiles).reshape(
                kernel_shape
            )
        x_ext = jnp.concatenate(
            [above[step_num][:, :own_rows], images[step_num, 0], below[step_num][:, :own_rows]],
            axis=1,
        )
        g_ext = jnp.concatenate(
            [above[step_num][:, own_rows:], out_grads[step_num, 0], below[step_num][:, own_rows:]],
            axis=1,
        )
        grads_chunk = scattered_sum(local_grads(x_ext, g_ext, weights, first, last), tiles)
        sum_state = sum_state - learn_rate * grads_chunk
        got = pushed(with_weight(sum_state, weight), peer_level)
        sum_state = 0.5 * (sum_state + got[:state_rows])
        weight = 0.5 * (weight + got[state_rows, 0])
    new_state = gathered(sum_state, tiles).reshape(kernel_shape)
    return (new_state[None], jnp.reshape(weight, (1,)))


def solution(mesh):
    in_specs = (
        P(None, "rep", None, "tile", None, None),
        P(None, "rep", None, "tile", None, None),
        P("rep", None, None, None),
        P("rep"),
        P(),
    )
    out_specs = (P("rep", None, None, None), P("rep"))
    return jax.shard_map(shards, mesh=mesh, in_specs=in_specs, out_specs=out_specs, check_vma=False)
```

```python
from functools import partial
import math

import jax
import jax.numpy as jnp
from jax import lax
from jax.sharding import PartitionSpec as P

learn_rate = 0.03


def passed_along(shard, axis, by):
    devices = lax.axis_size(axis)
    return lax.ppermute(shard, axis, [(i, (i + by) % devices) for i in range(devices)])


def pushed(payload, level):
    levels = lax.axis_size("rep").bit_length() - 1
    branches = [partial(passed_along, axis="rep", by=1 << bit_num) for bit_num in range(levels)]
    return lax.switch(level, branches, payload)


def conv_rows(field, kernel):
    channels = kernel.shape[1]
    return lax.conv_general_dilated(
        field,
        kernel.reshape(3, 3, channels, channels),
        (1, 1),
        ((0, 0), (1, 1)),
        dimension_numbers=("NHWC", "HWIO", "NHWC"),
        preferred_element_type=jnp.float32,
    )


def flipped(kernel):
    channels = kernel.shape[1]
    return (
        kernel.reshape(3, 3, channels, channels)[::-1, ::-1]
        .transpose(0, 1, 3, 2)
        .reshape(9 * channels, channels)
    )


def kernel_grad(field, cotangent):
    padded = jnp.pad(field, ((0, 0), (0, 0), (1, 1), (0, 0)))
    out = lax.conv_general_dilated(
        padded,
        cotangent,
        (1, 1),
        "VALID",
        dimension_numbers=("CHWN", "IHWO", "NHWC"),
        preferred_element_type=jnp.float32,
    )
    return out.transpose(1, 2, 0, 3).reshape(-1, cotangent.shape[-1])


def halo_rows(images, out_grads):
    tiles = lax.axis_size("tile")
    own_rows = images.shape[2]
    for_below = jnp.concatenate([images[0], out_grads[0, :, own_rows - 1 :]], axis=1)
    for_above = jnp.concatenate([images[0], out_grads[0, :, :1]], axis=1)
    down = [(i, i + 1) for i in range(tiles - 1)]
    up = [(i + 1, i) for i in range(tiles - 1)]
    return lax.ppermute(for_below, "tile", down), lax.ppermute(for_above, "tile", up)


def local_grads(x_ext, g_ext, weights, first, last):
    channels = x_ext.shape[-1]
    own_rows = x_ext.shape[1] - 4
    norm_scale = 1.0 / math.sqrt(9 * channels)
    pre_ext = norm_scale * conv_rows(x_ext, weights[0])
    row_ids = lax.broadcasted_iota(jnp.int32, (1, own_rows + 2, 1, 1), 1)
    outside = ((row_ids == 0) & first) | ((row_ids == own_rows + 1) & last)
    hidden_ext = jnp.where(outside, 0.0, jax.nn.silu(pre_ext)).astype(jnp.bfloat16)
    pre_act = pre_ext[:, 1 : own_rows + 1]
    grad_hidden = norm_scale * conv_rows(g_ext, flipped(weights[1]))
    sigmoid_val = jax.nn.sigmoid(pre_act)
    grad_pre = (grad_hidden * sigmoid_val * (1.0 + pre_act * (1.0 - sigmoid_val))).astype(
        jnp.bfloat16
    )
    grad_own = g_ext[:, 1 : own_rows + 1]
    first_grad = norm_scale * kernel_grad(x_ext[:, 1 : own_rows + 3], grad_pre)
    second = norm_scale * kernel_grad(hidden_ext, grad_own)
    return jnp.stack([first_grad, second])


def scattered_sum(grads, tiles):
    chunks = grads.astype(jnp.bfloat16).reshape(tiles, -1, grads.shape[-1])
    got = lax.all_to_all(chunks, "tile", 0, 0, tiled=True)
    return got.astype(jnp.float32).sum(0)


def gathered(chunk, tiles):
    spread = jnp.broadcast_to(chunk[None], (tiles,) + chunk.shape)
    return lax.all_to_all(spread, "tile", 0, 0, tiled=True)


def with_weight(chunk, weight):
    return jnp.concatenate([chunk, jnp.broadcast_to(weight, (1, chunk.shape[-1]))], axis=0)


def shards(images, out_grads, numerators, push_weight, step_index):
    levels = lax.axis_size("rep").bit_length() - 1
    tiles = lax.axis_size("tile")
    tile = lax.axis_index("tile")
    first, last = tile == 0, tile == tiles - 1
    kernel_shape = numerators.shape[1:]
    channels = kernel_shape[-1]
    full_state = numerators[0]
    state_rows = full_state.size // (tiles * channels)
    sum_state = full_state.reshape(tiles, state_rows, channels)[tile]
    weight = push_weight[0]
    own_rows = images.shape[3]
    for step_num in range(images.shape[0]):
        peer_level = (step_index[0] + step_num) % levels
        if step_num == 0:
            weights = (full_state / weight).astype(jnp.bfloat16)
        else:
            weights = gathered((sum_state / weight).astype(jnp.bfloat16), tiles).reshape(
                kernel_shape
            )
        if step_num == 0:
            above, below = halo_rows(images[0], out_grads[0])
        else:
            above, below = halo_rows(*step_inputs)
        x_ext = jnp.concatenate(
            [above[:, :own_rows], images[step_num, 0], below[:, :own_rows]], axis=1
        )
        g_ext = jnp.concatenate(
            [above[:, own_rows:], out_grads[step_num, 0], below[:, own_rows:]], axis=1
        )
        grads = local_grads(x_ext, g_ext, weights, first, last)
        if step_num + 1 < images.shape[0]:
            grads, *step_inputs = lax.optimization_barrier(
                (grads, images[step_num + 1], out_grads[step_num + 1])
            )
        grads_chunk = scattered_sum(grads, tiles)
        sum_state = sum_state - learn_rate * grads_chunk
        got = pushed(with_weight(sum_state, weight), peer_level)
        sum_state = 0.5 * (sum_state + got[:state_rows])
        weight = 0.5 * (weight + got[state_rows, 0])
    new_state = gathered(sum_state, tiles).reshape(kernel_shape)
    return (new_state[None], jnp.reshape(weight, (1,)))


def solution(mesh):
    in_specs = (
        P(None, "rep", None, "tile", None, None),
        P(None, "rep", None, "tile", None, None),
        P("rep", None, None, None),
        P("rep"),
        P(),
    )
    out_specs = (P("rep", None, None, None), P("rep"))
    return jax.shard_map(shards, mesh=mesh, in_specs=in_specs, out_specs=out_specs, check_vma=False)
```

```python
from functools import partial
import math

import jax
import jax.numpy as jnp
from jax import lax
from jax.sharding import PartitionSpec as P

learn_rate = 0.03


def passed_along(shard, axis, by):
    devices = lax.axis_size(axis)
    return lax.ppermute(shard, axis, [(i, (i + by) % devices) for i in range(devices)])


def pushed(payload, level):
    levels = lax.axis_size("rep").bit_length() - 1
    branches = [partial(passed_along, axis="rep", by=1 << bit_num) for bit_num in range(levels)]
    return lax.switch(level, branches, payload)


def conv_rows(field, kernel):
    channels = kernel.shape[1]
    return lax.conv_general_dilated(
        field,
        kernel.reshape(3, 3, channels, channels),
        (1, 1),
        ((0, 0), (1, 1)),
        dimension_numbers=("NHWC", "HWIO", "NHWC"),
        preferred_element_type=jnp.float32,
    )


def flipped(kernel):
    channels = kernel.shape[1]
    return (
        kernel.reshape(3, 3, channels, channels)[::-1, ::-1]
        .transpose(0, 1, 3, 2)
        .reshape(9 * channels, channels)
    )


def kernel_grad(field, cotangent):
    padded = jnp.pad(field, ((0, 0), (0, 0), (1, 1), (0, 0)))
    out = lax.conv_general_dilated(
        padded,
        cotangent,
        (1, 1),
        "VALID",
        dimension_numbers=("CHWN", "IHWO", "NHWC"),
        preferred_element_type=jnp.float32,
    )
    return out.transpose(1, 2, 0, 3).reshape(-1, cotangent.shape[-1])


def halo_rows(images, out_grads):
    tiles = lax.axis_size("tile")
    own_rows = images.shape[2]
    for_below = jnp.concatenate([images[0], out_grads[0, :, own_rows - 1 :]], axis=1)
    for_above = jnp.concatenate([images[0], out_grads[0, :, :1]], axis=1)
    down = [(i, i + 1) for i in range(tiles - 1)]
    up = [(i + 1, i) for i in range(tiles - 1)]
    return lax.ppermute(for_below, "tile", down), lax.ppermute(for_above, "tile", up)


def local_grads(x_ext, g_ext, weights, first, last):
    channels = x_ext.shape[-1]
    own_rows = x_ext.shape[1] - 4
    norm_scale = 1.0 / math.sqrt(9 * channels)
    pre_ext = norm_scale * conv_rows(x_ext, weights[0])
    row_ids = lax.broadcasted_iota(jnp.int32, (1, own_rows + 2, 1, 1), 1)
    outside = ((row_ids == 0) & first) | ((row_ids == own_rows + 1) & last)
    hidden_ext = jnp.where(outside, 0.0, jax.nn.silu(pre_ext)).astype(jnp.bfloat16)
    pre_act = pre_ext[:, 1 : own_rows + 1]
    grad_hidden = norm_scale * conv_rows(g_ext, flipped(weights[1]))
    sigmoid_val = jax.nn.sigmoid(pre_act)
    grad_pre = (grad_hidden * sigmoid_val * (1.0 + pre_act * (1.0 - sigmoid_val))).astype(
        jnp.bfloat16
    )
    grad_own = g_ext[:, 1 : own_rows + 1]
    first_grad = norm_scale * kernel_grad(x_ext[:, 1 : own_rows + 3], grad_pre)
    second = norm_scale * kernel_grad(hidden_ext, grad_own)
    return jnp.stack([first_grad, second])


def scattered_sum(grads, tiles):
    chunks = grads.astype(jnp.bfloat16).reshape(tiles, -1, grads.shape[-1])
    got = lax.all_to_all(chunks, "tile", 0, 0, tiled=True)
    return got.astype(jnp.float32).sum(0)


def gathered(chunk, tiles):
    spread = jnp.broadcast_to(chunk[None], (tiles,) + chunk.shape)
    return lax.all_to_all(spread, "tile", 0, 0, tiled=True)


def with_weight(chunk, weight):
    high = weight.astype(jnp.bfloat16)
    rest = weight - high.astype(jnp.float32)
    middle = rest.astype(jnp.bfloat16)
    low = (rest - middle.astype(jnp.float32)).astype(jnp.bfloat16)
    parts = jnp.zeros((1, chunk.shape[-1]), jnp.bfloat16).at[0, :3].set(jnp.stack([high, middle, low]))
    return jnp.concatenate([chunk.astype(jnp.bfloat16), parts], axis=0)


def weight_of(row):
    parts = row.astype(jnp.float32)
    return parts[0] + (parts[1] + parts[2])


def shards(images, out_grads, numerators, push_weight, step_index):
    levels = lax.axis_size("rep").bit_length() - 1
    tiles = lax.axis_size("tile")
    tile = lax.axis_index("tile")
    first, last = tile == 0, tile == tiles - 1
    kernel_shape = numerators.shape[1:]
    channels = kernel_shape[-1]
    full_state = numerators[0]
    state_rows = full_state.size // (tiles * channels)
    sum_state = full_state.reshape(tiles, state_rows, channels)[tile]
    weight = push_weight[0]
    own_rows = images.shape[3]
    for step_num in range(images.shape[0]):
        peer_level = (step_index[0] + step_num) % levels
        if step_num == 0:
            weights = (full_state / weight).astype(jnp.bfloat16)
        else:
            weights = gathered((sum_state / weight).astype(jnp.bfloat16), tiles).reshape(
                kernel_shape
            )
        if step_num == 0:
            above, below = halo_rows(images[0], out_grads[0])
        else:
            above, below = halo_rows(*step_inputs)
        x_ext = jnp.concatenate(
            [above[:, :own_rows], images[step_num, 0], below[:, :own_rows]], axis=1
        )
        g_ext = jnp.concatenate(
            [above[:, own_rows:], out_grads[step_num, 0], below[:, own_rows:]], axis=1
        )
        grads = local_grads(x_ext, g_ext, weights, first, last)
        if step_num + 1 < images.shape[0]:
            grads, *step_inputs = lax.optimization_barrier(
                (grads, images[step_num + 1], out_grads[step_num + 1])
            )
        grads_chunk = scattered_sum(grads, tiles)
        sum_state = sum_state - learn_rate * grads_chunk
        got = pushed(with_weight(sum_state, weight), peer_level)
        sum_state = 0.5 * (sum_state + got[:state_rows].astype(jnp.float32))
        weight = 0.5 * (weight + weight_of(got[state_rows]))
    new_state = gathered(sum_state, tiles).reshape(kernel_shape)
    return (new_state[None], jnp.reshape(weight, (1,)))


def solution(mesh):
    in_specs = (
        P(None, "rep", None, "tile", None, None),
        P(None, "rep", None, "tile", None, None),
        P("rep", None, None, None),
        P("rep"),
        P(),
    )
    out_specs = (P("rep", None, None, None), P("rep"))
    return jax.shard_map(shards, mesh=mesh, in_specs=in_specs, out_specs=out_specs, check_vma=False)
```

```python
from functools import partial
import math

import jax
import jax.numpy as jnp
from jax import lax
from jax.sharding import PartitionSpec as P

learn_rate = 0.03


def passed_along(shard, axis, by):
    devices = lax.axis_size(axis)
    return lax.ppermute(shard, axis, [(i, (i + by) % devices) for i in range(devices)])


def pushed(payload, level):
    levels = lax.axis_size("rep").bit_length() - 1
    branches = [partial(passed_along, axis="rep", by=1 << bit_num) for bit_num in range(levels)]
    return lax.switch(level, branches, payload)


def conv_rows(field, kernel):
    channels = kernel.shape[1]
    return lax.conv_general_dilated(
        field,
        kernel.reshape(3, 3, channels, channels),
        (1, 1),
        ((0, 0), (1, 1)),
        dimension_numbers=("NHWC", "HWIO", "NHWC"),
        preferred_element_type=jnp.float32,
    )


def flipped(kernel):
    channels = kernel.shape[1]
    return (
        kernel.reshape(3, 3, channels, channels)[::-1, ::-1]
        .transpose(0, 1, 3, 2)
        .reshape(9 * channels, channels)
    )


def kernel_grad(field, cotangent):
    padded = jnp.pad(field, ((0, 0), (0, 0), (1, 1), (0, 0)))
    out = lax.conv_general_dilated(
        padded,
        cotangent,
        (1, 1),
        "VALID",
        dimension_numbers=("CHWN", "IHWO", "NHWC"),
        preferred_element_type=jnp.float32,
    )
    return out.transpose(1, 2, 0, 3).reshape(-1, cotangent.shape[-1])


def halo_rows(images, out_grads):
    tiles = lax.axis_size("tile")
    own_rows = images.shape[2]
    for_below = jnp.concatenate([images[0], out_grads[0, :, own_rows - 1 :]], axis=1)
    for_above = jnp.concatenate([images[0], out_grads[0, :, :1]], axis=1)
    down = [(i, i + 1) for i in range(tiles - 1)]
    up = [(i + 1, i) for i in range(tiles - 1)]
    return lax.ppermute(for_below, "tile", down), lax.ppermute(for_above, "tile", up)


def local_grads(x_ext, g_ext, weights, first, last):
    channels = x_ext.shape[-1]
    own_rows = x_ext.shape[1] - 4
    norm_scale = 1.0 / math.sqrt(9 * channels)
    pre_ext = norm_scale * conv_rows(x_ext, weights[0])
    row_ids = lax.broadcasted_iota(jnp.int32, (1, own_rows + 2, 1, 1), 1)
    outside = ((row_ids == 0) & first) | ((row_ids == own_rows + 1) & last)
    hidden_ext = jnp.where(outside, 0.0, jax.nn.silu(pre_ext)).astype(jnp.bfloat16)
    pre_act = pre_ext[:, 1 : own_rows + 1]
    grad_hidden = norm_scale * conv_rows(g_ext, flipped(weights[1]))
    sigmoid_val = jax.nn.sigmoid(pre_act)
    grad_pre = (grad_hidden * sigmoid_val * (1.0 + pre_act * (1.0 - sigmoid_val))).astype(
        jnp.bfloat16
    )
    grad_own = g_ext[:, 1 : own_rows + 1]
    first_grad = norm_scale * kernel_grad(x_ext[:, 1 : own_rows + 3], grad_pre)
    second = norm_scale * kernel_grad(hidden_ext, grad_own)
    return jnp.stack([first_grad, second])


def scattered_sum(grads, tiles):
    chunks = grads.astype(jnp.bfloat16).reshape(tiles, -1, grads.shape[-1])
    got = lax.all_to_all(chunks, "tile", 0, 0, tiled=True)
    return got.astype(jnp.float32).sum(0)


def gathered(chunk, tiles):
    spread = jnp.broadcast_to(chunk[None], (tiles,) + chunk.shape)
    return lax.all_to_all(spread, "tile", 0, 0, tiled=True)


def with_weight(chunk, weight):
    high = weight.astype(jnp.bfloat16)
    rest = weight - high.astype(jnp.float32)
    middle = rest.astype(jnp.bfloat16)
    low = (rest - middle.astype(jnp.float32)).astype(jnp.bfloat16)
    parts = jnp.zeros((1, chunk.shape[-1]), jnp.bfloat16).at[0, :3].set(jnp.stack([high, middle, low]))
    return jnp.concatenate([chunk.astype(jnp.bfloat16), parts], axis=0)


def weight_of(row):
    parts = row.astype(jnp.float32)
    return parts[0] + (parts[1] + parts[2])


def shards(images, out_grads, numerators, push_weight, step_index):
    levels = lax.axis_size("rep").bit_length() - 1
    tiles = lax.axis_size("tile")
    tile = lax.axis_index("tile")
    first, last = tile == 0, tile == tiles - 1
    kernel_shape = numerators.shape[1:]
    channels = kernel_shape[-1]
    full_state = numerators[0]
    state_rows = full_state.size // (tiles * channels)
    sum_state = full_state.reshape(tiles, state_rows, channels)[tile]
    weight = push_weight[0]
    own_rows = images.shape[3]
    for step_num in range(images.shape[0]):
        peer_level = (step_index[0] + step_num) % levels
        if step_num == 0:
            weights = (full_state / weight).astype(jnp.bfloat16)
        else:
            weights = gathered((sum_state / weight).astype(jnp.bfloat16), tiles).reshape(
                kernel_shape
            )
        if step_num == 0:
            above, below = halo_rows(images[0], out_grads[0])
        else:
            above, below = halo_rows(*step_inputs)
        x_ext = jnp.concatenate(
            [above[:, :own_rows], images[step_num, 0], below[:, :own_rows]], axis=1
        )
        g_ext = jnp.concatenate(
            [above[:, own_rows:], out_grads[step_num, 0], below[:, own_rows:]], axis=1
        )
        grads = local_grads(x_ext, g_ext, weights, first, last)
        if step_num + 1 < images.shape[0]:
            grads, *step_inputs = lax.optimization_barrier(
                (grads, images[step_num + 1], out_grads[step_num + 1])
            )
        grads_chunk = scattered_sum(grads, tiles)
        sum_state = sum_state - learn_rate * grads_chunk
        got = pushed(with_weight(sum_state, weight), peer_level)
        sum_state = 0.5 * (sum_state + got[:state_rows].astype(jnp.float32))
        weight = 0.5 * (weight + weight_of(got[state_rows]))
    new_state = gathered(sum_state.astype(jnp.bfloat16), tiles).reshape(kernel_shape)
    new_state = new_state.astype(jnp.float32)
    return (new_state[None], jnp.reshape(weight, (1,)))


def solution(mesh):
    in_specs = (
        P(None, "rep", None, "tile", None, None),
        P(None, "rep", None, "tile", None, None),
        P("rep", None, None, None),
        P("rep"),
        P(),
    )
    out_specs = (P("rep", None, None, None), P("rep"))
    return jax.shard_map(shards, mesh=mesh, in_specs=in_specs, out_specs=out_specs, check_vma=False)
```
